256 devices in a mesh: user: 16 (over z, core), item: 16 (over y, x).
Axes of the slice: x: 4, y: 4, z: 8, core: 2. Of those that a mesh axis runs over, the one named last changes fastest.
Arguments:
- ratings: bfloat16 [30720, 128, 128], P(('user', 'item')), may hold values from -6 to 6
- weights: bfloat16 [30720, 128, 128], P(('user', 'item')), may hold values from 0.19921875 to 2
- row_masks: int32 [30720, 4], P(('user', 'item')), may hold values from -2147483648 to 2147483646
- tile_users: int32 [30720], P(('user', 'item')), may hold values from 0 to 15
- tile_items: int32 [30720], P(('user', 'item')), may hold values from 0 to 15
- tile_counts: int32 [256], P(('user', 'item')), may hold values from 1 to 120
- users: float32 [32768, 128], P(('user', 'item')), may hold values from -1.8 to 1.8
- items: float32 [2048, 128], P('item'), may hold values from -1.8 to 1.8
Outputs:
- new_users: float32 [32768, 128], P(('user', 'item'))
- new_items: float32 [2048, 128], P('item')
The draws below stay inside these ranges and needn't reach their ends.
All inputs are finite; a program needn't handle non-finite values.
Results may differ from the reference program's by a relative error of at most 0.002.
Values may be sent and summed in bfloat16 or wider, within the bound.
No kernel may reach another device: no remote copies, remote signals or barrier semaphores. Data moves between devices by JAX's collectives and lax.ppermute only.
A program may use at most 64 MiB of HBM per device.

```python
import math
import jax
import jax.numpy as jnp
from jax import lax

TILE = 128
RANK = 128
STEPS = 2
UBD = 1
IBD = 1
TD = 120
UBG = 16
NIB = 16
USERS = 32768
ITEMS = 2048
SLOTS = 30720
N_USER = 16
N_ITEM = 16


def draw_row_masks(key, part):
    return jax.random.randint(key, (SLOTS, TILE // 32), -2147483648, 2147483647, dtype=jnp.int32)


def draw_tile_counts(key, part):
    key_one, key_two = jax.random.split(key)
    devices = N_USER * N_ITEM
    base_draw = jax.random.randint(key_one, (devices,), 0, TD, dtype=jnp.int32)
    counts = 1 + base_draw * base_draw // TD
    chosen = jax.random.randint(key_two, (), 0, devices, dtype=jnp.int32)
    return jnp.where(jnp.arange(devices, dtype=jnp.int32) == chosen, TD, counts).astype(jnp.int32)


def place_ends(values, own_key, least, largest):
    longest = values.shape.index(max(values.shape))
    spots = []
    for shift in (0, 1):
        where = [jax.random.randint(jax.random.fold_in(own_key, axis), (), 0, length) for axis, length in enumerate(values.shape)]
        where[longest] = (where[longest] + shift) % values.shape[longest]
        spots.append(tuple(where))
    return values.at[spots[0]].set(least).at[spots[1]].set(largest)


def block_levels(stream_key, dims, shards, least, top_value):
    level, own = 1.0, jax.random.fold_in(stream_key, 6)
    for position, shards_of in shards:
        draws = jnp.exp(jax.random.uniform(jax.random.fold_in(own, position), (shards_of,), jnp.float32, least / len(shards), top_value / len(shards)))
        level = level * jnp.repeat(draws, dims[position] // shards_of).reshape([-1 if axis == position else 1 for axis in range(len(dims))])
    return level


def bell_draw(key, shape, scale, limit, shards=(), kind=jnp.bfloat16):
    gain = block_levels(key, shape, shards, -0.22, 0.18) if shards else 1.0
    result = jax.random.normal(key, shape, jnp.float32) * scale * gain
    return jnp.minimum(jnp.maximum(result, -limit), limit).astype(kind)


def setup_inputs(seed: int = 0) -> dict:
    splits = jax.random.split(jax.random.key(seed), 9)
    ratings = bell_draw(splits[0], (SLOTS, TILE, TILE), 1.0, 6.0, ((0, 256),))
    weights = jnp.clip(jnp.exp(math.log(2.0) - 2.306499 * jax.random.uniform(splits[1], (SLOTS, TILE, TILE), jnp.float32) ** block_levels(splits[1], (SLOTS, TILE, TILE), ((0, 256),), -0.2, 0.2)), 0.19921875, 2.0).astype(jnp.bfloat16)
    row_masks = draw_row_masks(jax.random.fold_in(splits[8], 71), 0)
    tile_users = place_ends(jax.random.randint(splits[3], (SLOTS,), 0, UBG), jax.random.fold_in(splits[3], 1), 0, UBG - 1).astype(jnp.int32)
    tile_items = place_ends(jax.random.randint(splits[4], (SLOTS,), 0, NIB), jax.random.fold_in(splits[4], 1), 0, NIB - 1).astype(jnp.int32)
    tile_counts = draw_tile_counts(jax.random.fold_in(splits[8], 71), 0)
    users = bell_draw(splits[6], (USERS, RANK), 0.3, 1.8, ((0, 256),), jnp.float32)
    items = bell_draw(splits[7], (ITEMS, RANK), 0.3, 1.8, ((0, 16),), jnp.float32)
    return dict(ratings=ratings, weights=weights, row_masks=row_masks, tile_users=tile_users, tile_items=tile_items, tile_counts=tile_counts, users=users, items=items)


STEP_SCALE = 4.0
DECAY_RATE = 0.02


def unpack_rows(packed, side):
    lanes = jnp.arange(side, dtype=jnp.int32)
    picked = packed[:, lanes // 32]
    return jnp.bitwise_and(jnp.right_shift(picked, lanes % 32), 1)


def reference(ratings, weights, row_masks, tile_users, tile_items, tile_counts, users, items):
    devices = N_USER * N_ITEM
    user_blocks = UBD * N_ITEM
    all_blocks = N_USER * user_blocks
    item_blocks = IBD * N_ITEM
    shaped = (ratings.reshape(devices, TD, TILE, TILE),
              weights.reshape(devices, TD, TILE, TILE),
              row_masks.reshape(devices, TD, TILE // 32),
              tile_users.reshape(devices, TD),
              tile_items.reshape(devices, TD),
              tile_counts,
              jnp.arange(devices, dtype=jnp.int32))
    for iteration in range(STEPS):
        user_half = lax.optimization_barrier(users.astype(jnp.bfloat16)).astype(jnp.float32).reshape(all_blocks, TILE, RANK)
        item_half = lax.optimization_barrier(items.astype(jnp.bfloat16)).astype(jnp.float32).reshape(item_blocks, TILE, RANK)

        def per_device(totals, pieces):
            user_sum, user_diag, item_sum, item_diag = totals
            tile_vals, tile_wts, packed, local_users, item_ids, tile_count, device = pieces
            group_ids = ((device // N_ITEM) * user_blocks + local_users).astype(jnp.int32)
            live_slots = (jnp.arange(TD, dtype=jnp.int32) < tile_count).astype(jnp.float32)
            rowbits = unpack_rows(packed, TILE).astype(jnp.float32) * live_slots[:, None]
            weighted = tile_wts.astype(jnp.float32) * rowbits[:, :, None]
            user_rows = user_half[group_ids]
            item_rows = item_half[item_ids]
            predicted = jnp.einsum("tbr,tcr->tbc", user_rows, item_rows)
            residual = weighted * (tile_vals.astype(jnp.float32) - predicted)
            residual = lax.optimization_barrier(residual.astype(jnp.bfloat16)).astype(jnp.float32)
            user_part = jnp.einsum("tbc,tcr->tbr", residual, item_rows)
            item_part = jnp.einsum("tbc,tbr->tcr", residual, user_rows)
            user_sum = user_sum.at[group_ids].add(user_part)
            user_diag = user_diag.at[group_ids].add(jnp.sum(weighted, axis=2))
            item_sum = item_sum.at[item_ids].add(item_part)
            item_diag = item_diag.at[item_ids].add(jnp.sum(weighted, axis=1))
            return (user_sum, user_diag, item_sum, item_diag), None

        start_totals = (jnp.zeros((all_blocks, TILE, RANK), jnp.float32),
                        jnp.zeros((all_blocks, TILE), jnp.float32),
                        jnp.zeros((item_blocks, TILE, RANK), jnp.float32),
                        jnp.zeros((item_blocks, TILE), jnp.float32))
        totals, unused = lax.scan(per_device, start_totals, shaped)
        user_sum, user_diag, item_sum, item_diag = totals
        user_weight = 2.0 * TILE + user_diag.reshape(-1)
        item_weight = 2.0 * TILE + item_diag.reshape(-1)
        users = users + STEP_SCALE * (user_sum.reshape(-1, RANK) / user_weight[:, None] - DECAY_RATE * users)
        items = items + STEP_SCALE * (item_sum.reshape(-1, RANK) / item_weight[:, None] - DECAY_RATE * items)
    return users, items
```

```python
import functools

import jax
import jax.numpy as jnp
from jax import lax
from jax.experimental import pallas as pl
from jax.experimental.pallas import tpu as pltpu
from jax.sharding import PartitionSpec as P

STEPS = 2


STEP_SCALE = 4.0
DECAY_RATE = 0.02

PER_BLOCK = 8


def tile_kernel(with_diag, per_block, count_ref, users_ref, items_ref, masks_ref,
                panel_ref, ratings_ref, weights_ref, acc_ref):
    step = pl.program_id(0)
    side = ratings_ref.shape[1]
    f32, bf16 = jnp.float32, jnp.bfloat16

    @pl.when(step == 0)
    def _():
        acc_ref[...] = jnp.zeros_like(acc_ref)

    count = count_ref[0]
    rows = lax.broadcasted_iota(jnp.int32, (side, side), 0)
    shift = jnp.bitwise_and(rows, 31)
    word_of = jnp.right_shift(rows, 5)
    if with_diag:
        picks = lax.broadcasted_iota(jnp.int32, (8, side), 0)
        first_row = (picks == 0).astype(bf16)
        second_row = (picks == 1).astype(bf16)

    for k in range(per_block):
        slot = step * per_block + k

        @pl.when(slot < count)
        def _():
            ub = users_ref[slot]
            ib = items_ref[slot]
            words = [masks_ref[slot * 4 + q] for q in range(4)]
            word = jnp.where(word_of == 0, words[0],
                             jnp.where(word_of == 1, words[1],
                                       jnp.where(word_of == 2, words[2], words[3])))
            bit = jnp.bitwise_and(lax.shift_right_logical(word, shift), 1)
            weighted = weights_ref[k].astype(f32) * bit.astype(f32)
            user_rows = panel_ref[ub, 0:side, :]
            item_rows = panel_ref[ib, side:2 * side, :]
            predicted = lax.dot_general(user_rows, item_rows, (((1,), (1,)), ((), ())),
                                        preferred_element_type=f32)
            residual = (weighted * (ratings_ref[k].astype(f32) - predicted)).astype(bf16)
            acc_ref[ub, 0:side, :] += jnp.dot(residual, item_rows, preferred_element_type=f32)
            acc_ref[ib, side:2 * side, :] += lax.dot_general(
                residual, user_rows, (((0,), (0,)), ((), ())), preferred_element_type=f32)
            if with_diag:
                half = weighted.astype(bf16)
                acc_ref[ub, 2 * side:2 * side + 8, :] += lax.dot_general(
                    first_row, half, (((1,), (1,)), ((), ())), preferred_element_type=f32)
                acc_ref[ib, 2 * side:2 * side + 8, :] += jnp.dot(
                    second_row, half, preferred_element_type=f32)


def tile_terms(with_diag, blocks, count, tile_users, tile_items, masks, panel, ratings, weights):
    slots, side, _ = ratings.shape
    per_block = PER_BLOCK
    grid = slots // per_block
    acc_rows = 2 * side + (8 if with_diag else 0)

    def tile_map(step, count_ref, *_):
        last = jnp.maximum((count_ref[0] - 1) // per_block, 0)
        return (jnp.minimum(step, last), 0, 0)

    def whole(step, *_):
        return (0, 0, 0)

    flops = slots * (3 * 2 * side * side * side)
    bytes_accessed = 2 * ratings.size * 2 + panel.size * 2 + blocks * acc_rows * side * 4
    return pl.pallas_call(
        functools.partial(tile_kernel, with_diag, per_block),
        out_shape=jax.ShapeDtypeStruct((blocks, acc_rows, side), jnp.float32),
        grid_spec=pltpu.PrefetchScalarGridSpec(
            num_scalar_prefetch=4,
            grid=(grid,),
            in_specs=[
                pl.BlockSpec(panel.shape, whole),
                pl.BlockSpec((per_block, side, side), tile_map),
                pl.BlockSpec((per_block, side, side), tile_map),
            ],
            out_specs=pl.BlockSpec((blocks, acc_rows, side), whole),
        ),
        compiler_params=pltpu.CompilerParams(dimension_semantics=("arbitrary",)),
        cost_estimate=pl.CostEstimate(flops=flops, bytes_accessed=bytes_accessed, transcendentals=0),
    )(count, tile_users, tile_items, masks, panel, ratings, weights)


def gather_panel(users, items, blocks):
    own = jnp.concatenate([users.astype(jnp.bfloat16), items.astype(jnp.bfloat16)], axis=0)
    copies = jnp.broadcast_to(own[None], (blocks,) + own.shape)
    return lax.all_to_all(copies, "item", 0, 0, tiled=False)


def sum_over_user(part, groups):
    copies = jnp.broadcast_to(part[None], (groups,) + part.shape)
    return jnp.sum(lax.all_to_all(copies, "user", 0, 0, tiled=False), axis=0)


def on_device(groups, blocks, ratings, weights, row_masks, tile_users, tile_items, tile_counts, users, items):
    side = ratings.shape[1]
    masks = row_masks.reshape(-1)
    user_weight = None
    item_weight = None
    for iteration in range(STEPS):
        with_diag = iteration == 0
        panel = gather_panel(users, items, blocks)
        acc = tile_terms(with_diag, blocks, tile_counts, tile_users, tile_items, masks, panel, ratings, weights)
        total = jnp.sum(lax.all_to_all(acc, "item", 0, 0, tiled=False), axis=0)
        item_total = sum_over_user(total[side:], groups)
        user_grad = total[0:side]
        item_grad = item_total[0:side]
        if with_diag:
            user_weight = 2.0 * side + total[2 * side]
            item_weight = 2.0 * side + item_total[side + 1]
        users = users + STEP_SCALE * (user_grad / user_weight[:, None] - DECAY_RATE * users)
        items = items + STEP_SCALE * (item_grad / item_weight[:, None] - DECAY_RATE * items)
    return (users, items)


def solution(mesh):
    groups = mesh.shape["user"]
    blocks = mesh.shape["item"]
    return jax.shard_map(
        functools.partial(on_device, groups, blocks),
        mesh=mesh,
        in_specs=(
            P(("user", "item"), None, None),
            P(("user", "item"), None, None),
            P(("user", "item"), None),
            P(("user", "item")),
            P(("user", "item")),
            P(("user", "item")),
            P(("user", "item"), None),
            P("item", None),
        ),
        out_specs=(P(("user", "item"), None), P("item", None)),
        check_vma=False,
    )
```

```python
import functools

import jax
import jax.numpy as jnp
from jax import lax
from jax.experimental import pallas as pl
from jax.experimental.pallas import tpu as pltpu
from jax.sharding import PartitionSpec as P

STEPS = 2


STEP_SCALE = 4.0
DECAY_RATE = 0.02

PER_BLOCK = 24


def tile_kernel(with_diag, per_block, count_ref, users_ref, items_ref, masks_ref,
                panel_ref, ratings_ref, weights_ref, acc_ref):
    step = pl.program_id(0)
    side = ratings_ref.shape[1]
    f32, bf16 = jnp.float32, jnp.bfloat16

    @pl.when(step == 0)
    def _():
        acc_ref[...] = jnp.zeros_like(acc_ref)

    count = count_ref[0]

    @pl.when(step * per_block < count)
    def _():
        rows = lax.broadcasted_iota(jnp.int32, (side, side), 0)
        shift = jnp.bitwise_and(rows, 31)
        word_of = jnp.right_shift(rows, 5)
        if with_diag:
            picks = lax.broadcasted_iota(jnp.int32, (8, side), 0)
            first_row = (picks == 0).astype(bf16)
            second_row = (picks == 1).astype(bf16)
        for k in range(per_block):
            slot = step * per_block + k
            ub = users_ref[slot]
            ib = items_ref[slot]
            words = [masks_ref[slot * 4 + q] for q in range(4)]
            word = jnp.where(word_of == 0, words[0],
                             jnp.where(word_of == 1, words[1],
                                       jnp.where(word_of == 2, words[2], words[3])))
            bit = jnp.bitwise_and(lax.shift_right_logical(word, shift), 1)
            live = (slot < count).astype(f32)
            weighted = weights_ref[k].astype(f32) * (bit.astype(f32) * live)
            user_rows = panel_ref[ub, 0:side, :]
            item_rows = panel_ref[ib, side:2 * side, :]
            user_cols = panel_ref[ub, 2 * side:3 * side, :]
            item_cols = panel_ref[ib, 3 * side:4 * side, :]
            predicted = jnp.dot(user_rows, item_cols, preferred_element_type=f32)
            residual = (weighted * (ratings_ref[k].astype(f32) - predicted)).astype(bf16)
            acc_ref[ub, 0:side, :] += jnp.dot(residual, item_rows, preferred_element_type=f32)
            acc_ref[ib, side:2 * side, :] += jnp.dot(user_cols, residual, preferred_element_type=f32)
            if with_diag:
                half = weighted.astype(bf16)
                acc_ref[ub, 2 * side:2 * side + 8, :] += lax.dot_general(
                    first_row, half, (((1,), (1,)), ((), ())), preferred_element_type=f32)
                acc_ref[ib, 2 * side:2 * side + 8, :] += jnp.dot(
                    second_row, half, preferred_element_type=f32)


def tile_terms(with_diag, blocks, count, tile_users, tile_items, masks, panel, ratings, weights):
    slots, side, _ = ratings.shape
    per_block = PER_BLOCK
    grid = slots // per_block
    acc_rows = 2 * side + (8 if with_diag else 0)

    def tile_map(step, count_ref, *_):
        last = jnp.maximum((count_ref[0] - 1) // per_block, 0)
        return (jnp.minimum(step, last), 0, 0)

    def whole(step, *_):
        return (0, 0, 0)

    flops = slots * (3 * 2 * side * side * side)
    bytes_accessed = 2 * ratings.size * 2 + panel.size * 2 + blocks * acc_rows * side * 4
    return pl.pallas_call(
        functools.partial(tile_kernel, with_diag, per_block),
        out_shape=jax.ShapeDtypeStruct((blocks, acc_rows, side), jnp.float32),
        grid_spec=pltpu.PrefetchScalarGridSpec(
            num_scalar_prefetch=4,
            grid=(grid,),
            in_specs=[
                pl.BlockSpec(panel.shape, whole),
                pl.BlockSpec((per_block, side, side), tile_map),
                pl.BlockSpec((per_block, side, side), tile_map),
            ],
            out_specs=pl.BlockSpec((blocks, acc_rows, side), whole),
        ),
        compiler_params=pltpu.CompilerParams(dimension_semantics=("arbitrary",)),
        cost_estimate=pl.CostEstimate(flops=flops, bytes_accessed=bytes_accessed, transcendentals=0),
    )(count, tile_users, tile_items, masks, panel, ratings, weights)


def gather_panel(users, items, blocks):
    own = jnp.concatenate([users.astype(jnp.bfloat16), items.astype(jnp.bfloat16)], axis=0)
    copies = jnp.broadcast_to(own[None], (blocks,) + own.shape)
    gathered = lax.all_to_all(copies, "item", 0, 0, tiled=False)
    return jnp.concatenate([gathered, jnp.swapaxes(gathered[:, :users.shape[0]], 1, 2),
                            jnp.swapaxes(gathered[:, users.shape[0]:], 1, 2)], axis=1)


def sum_over_user(part, groups):
    copies = jnp.broadcast_to(part[None], (groups,) + part.shape)
    return jnp.sum(lax.all_to_all(copies, "user", 0, 0, tiled=False), axis=0)


def on_device(groups, blocks, ratings, weights, row_masks, tile_users, tile_items, tile_counts, users, items):
    side = ratings.shape[1]
    masks = row_masks.reshape(-1)
    user_weight = None
    item_weight = None
    for iteration in range(STEPS):
        with_diag = iteration == 0
        panel = gather_panel(users, items, blocks)
        acc = tile_terms(with_diag, blocks, tile_counts, tile_users, tile_items, masks, panel, ratings, weights)
        total = jnp.sum(lax.all_to_all(acc, "item", 0, 0, tiled=False), axis=0)
        item_total = sum_over_user(total[side:], groups)
        user_grad = total[0:side]
        item_grad = item_total[0:side].T
        if with_diag:
            user_weight = 2.0 * side + total[2 * side]
            item_weight = 2.0 * side + item_total[side + 1]
        users = users + STEP_SCALE * (user_grad / user_weight[:, None] - DECAY_RATE * users)
        items = items + STEP_SCALE * (item_grad / item_weight[:, None] - DECAY_RATE * items)
    return (users, items)


def solution(mesh):
    groups = mesh.shape["user"]
    blocks = mesh.shape["item"]
    return jax.shard_map(
        functools.partial(on_device, groups, blocks),
        mesh=mesh,
        in_specs=(
            P(("user", "item"), None, None),
            P(("user", "item"), None, None),
            P(("user", "item"), None),
            P(("user", "item")),
            P(("user", "item")),
            P(("user", "item")),
            P(("user", "item"), None),
            P("item", None),
        ),
        out_specs=(P(("user", "item"), None), P("item", None)),
        check_vma=False,
    )
```

```python
import functools

import jax
import jax.numpy as jnp
from jax import lax
from jax.experimental import pallas as pl
from jax.experimental.pallas import tpu as pltpu
from jax.sharding import PartitionSpec as P

STEPS = 2


STEP_SCALE = 4.0
DECAY_RATE = 0.02

PER_BLOCK = 24


def tile_kernel(with_diag, per_block, count_ref, users_ref, items_ref, masks_ref,
                panel_ref, ratings_ref, weights_ref, acc_ref):
    step = pl.program_id(0)
    side = ratings_ref.shape[1]
    f32, bf16 = jnp.float32, jnp.bfloat16

    @pl.when(step == 0)
    def _():
        acc_ref[...] = jnp.zeros_like(acc_ref)

    count = count_ref[0]

    @pl.when(step * per_block < count)
    def _():
        rows = lax.broadcasted_iota(jnp.int32, (side, side), 0)
        shift = jnp.bitwise_and(rows, 31)
        word_of = jnp.right_shift(rows, 5)
        if with_diag:
            picks = lax.broadcasted_iota(jnp.int32, (8, side), 0)
            first_row = (picks == 0).astype(bf16)
            second_row = (picks == 1).astype(bf16)
        for k in range(per_block):
            slot = step * per_block + k
            ub = users_ref[slot]
            ib = items_ref[slot]
            words = [masks_ref[slot * 4 + q] for q in range(4)]
            word = jnp.where(word_of == 0, words[0],
                             jnp.where(word_of == 1, words[1],
                                       jnp.where(word_of == 2, words[2], words[3])))
            bit = jnp.bitwise_and(lax.shift_right_logical(word, shift), 1)
            live = (slot < count).astype(f32)
            weighted = weights_ref[k].astype(f32) * (bit.astype(f32) * live)
            user_rows = panel_ref[ub, 0:side, :]
            item_rows = panel_ref[ib, side:2 * side, :]
            user_cols = panel_ref[ub, 2 * side:3 * side, :]
            item_cols = panel_ref[ib, 3 * side:4 * side, :]
            predicted = jnp.dot(user_rows, item_cols, preferred_element_type=f32)
            residual = (weighted * (ratings_ref[k].astype(f32) - predicted)).astype(bf16)
            acc_ref[ub, 0:side, :] += jnp.dot(residual, item_rows, preferred_element_type=f32)
            acc_ref[ib, side:2 * side, :] += jnp.dot(user_cols, residual, preferred_element_type=f32)
            if with_diag:
                half = weighted.astype(bf16)
                acc_ref[ub, 2 * side:2 * side + 8, :] += lax.dot_general(
                    first_row, half, (((1,), (1,)), ((), ())), preferred_element_type=f32)
                acc_ref[ib, 2 * side:2 * side + 8, :] += jnp.dot(
                    second_row, half, preferred_element_type=f32)


def tile_terms(with_diag, blocks, count, tile_users, tile_items, masks, panel, ratings, weights):
    slots, side, _ = ratings.shape
    per_block = PER_BLOCK
    grid = slots // per_block
    acc_rows = 2 * side + (8 if with_diag else 0)

    def tile_map(step, count_ref, *_):
        last = jnp.maximum((count_ref[0] - 1) // per_block, 0)
        return (jnp.minimum(step, last), 0, 0)

    def whole(step, *_):
        return (0, 0, 0)

    flops = slots * (3 * 2 * side * side * side)
    bytes_accessed = 2 * ratings.size * 2 + panel.size * 2 + blocks * acc_rows * side * 4
    return pl.pallas_call(
        functools.partial(tile_kernel, with_diag, per_block),
        out_shape=jax.ShapeDtypeStruct((blocks, acc_rows, side), jnp.float32),
        grid_spec=pltpu.PrefetchScalarGridSpec(
            num_scalar_prefetch=4,
            grid=(grid,),
            in_specs=[
                pl.BlockSpec(panel.shape, whole),
                pl.BlockSpec((per_block, side, side), tile_map),
                pl.BlockSpec((per_block, side, side), tile_map),
            ],
            out_specs=pl.BlockSpec((blocks, acc_rows, side), whole),
        ),
        compiler_params=pltpu.CompilerParams(dimension_semantics=("arbitrary",)),
        cost_estimate=pl.CostEstimate(flops=flops, bytes_accessed=bytes_accessed, transcendentals=0),
    )(count, tile_users, tile_items, masks, panel, ratings, weights)


def gather_panel(users, items, blocks):
    own = jnp.concatenate([users.astype(jnp.bfloat16), items.astype(jnp.bfloat16)], axis=0)
    copies = jnp.broadcast_to(own[None], (blocks,) + own.shape)
    gathered = lax.all_to_all(copies, "item", 0, 0, tiled=False)
    return jnp.concatenate([gathered, jnp.swapaxes(gathered[:, :users.shape[0]], 1, 2),
                            jnp.swapaxes(gathered[:, users.shape[0]:], 1, 2)], axis=1)


def sum_over_user(part, groups):
    assert groups & (groups - 1) == 0
    distance = 1
    while distance < groups:
        pairs = [(j, j ^ distance) for j in range(groups)]
        part = part + lax.ppermute(part, "user", pairs)
        distance *= 2
    return part


def on_device(groups, blocks, ratings, weights, row_masks, tile_users, tile_items, tile_counts, users, items):
    side = ratings.shape[1]
    masks = row_masks.reshape(-1)
    user_weight = None
    item_weight = None
    for iteration in range(STEPS):
        with_diag = iteration == 0
        panel = gather_panel(users, items, blocks)
        acc = tile_terms(with_diag, blocks, tile_counts, tile_users, tile_items, masks, panel, ratings, weights)
        total = jnp.sum(lax.all_to_all(acc, "item", 0, 0, tiled=False), axis=0)
        item_total = sum_over_user(total[side:], groups)
        user_grad = total[0:side]
        item_grad = item_total[0:side].T
        if with_diag:
            user_weight = 2.0 * side + total[2 * side]
            item_weight = 2.0 * side + item_total[side + 1]
        users = users + STEP_SCALE * (user_grad / user_weight[:, None] - DECAY_RATE * users)
        items = items + STEP_SCALE * (item_grad / item_weight[:, None] - DECAY_RATE * items)
    return (users, items)


def solution(mesh):
    groups = mesh.shape["user"]
    blocks = mesh.shape["item"]
    return jax.shard_map(
        functools.partial(on_device, groups, blocks),
        mesh=mesh,
        in_specs=(
            P(("user", "item"), None, None),
            P(("user", "item"), None, None),
            P(("user", "item"), None),
            P(("user", "item")),
            P(("user", "item")),
            P(("user", "item")),
            P(("user", "item"), None),
            P("item", None),
        ),
        out_specs=(P(("user", "item"), None), P("item", None)),
        check_vma=False,
    )
```

```python
import functools

import jax
import jax.numpy as jnp
from jax import lax
from jax.experimental import pallas as pl
from jax.experimental.pallas import tpu as pltpu
from jax.sharding import PartitionSpec as P

STEPS = 2


STEP_SCALE = 4.0
DECAY_RATE = 0.02

PER_BLOCK = 24


def tile_kernel(with_diag, per_block, count_ref, users_ref, items_ref, *refs):
    if with_diag:
        panel_ref, ratings_ref, weighted_ref, diag_ref, acc_ref = refs
    else:
        panel_ref, ratings_ref, weighted_ref, acc_ref = refs
    step = pl.program_id(0)
    side = ratings_ref.shape[1]
    f32, bf16 = jnp.float32, jnp.bfloat16

    @pl.when(step == 0)
    def _():
        acc_ref[:, 0:2 * side, :] = jnp.zeros((acc_ref.shape[0], 2 * side, side), f32)
        if with_diag:
            acc_ref[:, 2 * side:, :] = diag_ref[...]

    count = count_ref[0]

    @pl.when(step * per_block < count)
    def _():
        for k in range(per_block):
            slot = step * per_block + k
            ub = users_ref[slot]
            ib = items_ref[slot]
            user_rows = panel_ref[ub, 0:side, :]
            item_rows = panel_ref[ib, side:2 * side, :]
            user_cols = panel_ref[ub, 2 * side:3 * side, :]
            item_cols = panel_ref[ib, 3 * side:4 * side, :]
            predicted = jnp.dot(user_rows, item_cols, preferred_element_type=f32)
            residual = (weighted_ref[k].astype(f32) * (ratings_ref[k].astype(f32) - predicted)).astype(bf16)
            acc_ref[ub, 0:side, :] += jnp.dot(residual, item_rows, preferred_element_type=f32)
            acc_ref[ib, side:2 * side, :] += jnp.dot(user_cols, residual, preferred_element_type=f32)


def tile_terms(blocks, count, tile_users, tile_items, panel, ratings, weighted, diag=None):
    with_diag = diag is not None
    slots, side, _ = ratings.shape
    per_block = PER_BLOCK
    grid = slots // per_block
    acc_rows = 2 * side + (diag.shape[1] if with_diag else 0)

    def tile_map(step, count_ref, *_):
        last = jnp.maximum((count_ref[0] - 1) // per_block, 0)
        return (jnp.minimum(step, last), 0, 0)

    def whole(step, *_):
        return (0, 0, 0)

    in_specs = [
        pl.BlockSpec(panel.shape, whole),
        pl.BlockSpec((per_block, side, side), tile_map),
        pl.BlockSpec((per_block, side, side), tile_map),
    ]
    operands = [panel, ratings, weighted]
    if with_diag:
        in_specs.append(pl.BlockSpec(diag.shape, whole))
        operands.append(diag)
    flops = slots * (3 * 2 * side * side * side)
    bytes_accessed = 2 * ratings.size * 2 + panel.size * 2 + blocks * acc_rows * side * 4
    return pl.pallas_call(
        functools.partial(tile_kernel, with_diag, per_block),
        out_shape=jax.ShapeDtypeStruct((blocks, acc_rows, side), jnp.float32),
        grid_spec=pltpu.PrefetchScalarGridSpec(
            num_scalar_prefetch=3,
            grid=(grid,),
            in_specs=in_specs,
            out_specs=pl.BlockSpec((blocks, acc_rows, side), whole),
        ),
        compiler_params=pltpu.CompilerParams(dimension_semantics=("arbitrary",)),
        cost_estimate=pl.CostEstimate(flops=flops, bytes_accessed=bytes_accessed, transcendentals=0),
    )(count, tile_users, tile_items, *operands)


def prepare(weights, row_masks, tile_users, tile_items, tile_counts, blocks):
    f32 = jnp.float32
    slots, side, _ = weights.shape
    lanes = jnp.arange(side, dtype=jnp.int32)
    bits = jnp.bitwise_and(jnp.right_shift(row_masks[:, lanes // 32], lanes % 32), 1)
    live = (jnp.arange(slots, dtype=jnp.int32) < tile_counts[0]).astype(f32)
    keep = bits.astype(f32) * live[:, None]
    weighted = weights.astype(f32) * keep[:, :, None]
    row_sums = jnp.sum(weighted, axis=2)
    col_sums = jnp.sum(weighted, axis=1)
    ids = jnp.arange(blocks, dtype=jnp.int32)[:, None]
    user_hot = (tile_users[None, :] == ids).astype(f32)
    item_hot = (tile_items[None, :] == ids).astype(f32)
    user_diag = jnp.dot(user_hot, row_sums, precision=lax.Precision.HIGHEST)
    item_diag = jnp.dot(item_hot, col_sums, precision=lax.Precision.HIGHEST)
    diag = jnp.concatenate([user_diag[:, None], item_diag[:, None], jnp.zeros((blocks, 6, side), f32)], axis=1)
    return weighted.astype(jnp.bfloat16), diag


def gather_panel(users, items, blocks):
    own = jnp.concatenate([users.astype(jnp.bfloat16), items.astype(jnp.bfloat16)], axis=0)
    copies = jnp.broadcast_to(own[None], (blocks,) + own.shape)
    gathered = lax.all_to_all(copies, "item", 0, 0, tiled=False)
    return jnp.concatenate([gathered, jnp.swapaxes(gathered[:, :users.shape[0]], 1, 2),
                            jnp.swapaxes(gathered[:, users.shape[0]:], 1, 2)], axis=1)


def sum_over_user(part, groups):
    assert groups & (groups - 1) == 0
    distance = 1
    while distance < groups:
        pairs = [(j, j ^ distance) for j in range(groups)]
        part = part + lax.ppermute(part, "user", pairs)
        distance *= 2
    return part


def on_device(groups, blocks, ratings, weights, row_masks, tile_users, tile_items, tile_counts, users, items):
    side = ratings.shape[1]
    weighted, diag = prepare(weights, row_masks, tile_users, tile_items, tile_counts, blocks)
    user_weight = None
    item_weight = None
    for iteration in range(STEPS):
        with_diag = iteration == 0
        panel = gather_panel(users, items, blocks)
        acc = tile_terms(blocks, tile_counts, tile_users, tile_items, panel, ratings, weighted,
                         diag if with_diag else None)
        total = jnp.sum(lax.all_to_all(acc, "item", 0, 0, tiled=False), axis=0)
        item_total = sum_over_user(total[side:], groups)
        user_grad = total[0:side]
        item_grad = item_total[0:side].T
        if with_diag:
            user_weight = 2.0 * side + total[2 * side]
            item_weight = 2.0 * side + item_total[side + 1]
        users = users + STEP_SCALE * (user_grad / user_weight[:, None] - DECAY_RATE * users)
        items = items + STEP_SCALE * (item_grad / item_weight[:, None] - DECAY_RATE * items)
    return (users, items)


def solution(mesh):
    groups = mesh.shape["user"]
    blocks = mesh.shape["item"]
    return jax.shard_map(
        functools.partial(on_device, groups, blocks),
        mesh=mesh,
        in_specs=(
            P(("user", "item"), None, None),
            P(("user", "item"), None, None),
            P(("user", "item"), None),
            P(("user", "item")),
            P(("user", "item")),
            P(("user", "item")),
            P(("user", "item"), None),
            P("item", None),
        ),
        out_specs=(P(("user", "item"), None), P("item", None)),
        check_vma=False,
    )
```

```python
import functools

import jax
import jax.numpy as jnp
from jax import lax
from jax.experimental import pallas as pl
from jax.experimental.pallas import tpu as pltpu
from jax.sharding import PartitionSpec as P

STEPS = 2


STEP_SCALE = 4.0
DECAY_RATE = 0.02

PER_BLOCK = 40


def tile_kernel(with_diag, per_block, count_ref, users_ref, items_ref, *refs):
    if with_diag:
        panel_ref, ratings_ref, weighted_ref, diag_ref, acc_ref, residual_ref = refs
    else:
        panel_ref, ratings_ref, weighted_ref, acc_ref, residual_ref = refs
    step = pl.program_id(0)
    side = ratings_ref.shape[1]
    f32, bf16 = jnp.float32, jnp.bfloat16

    @pl.when(step == 0)
    def _():
        acc_ref[:, 0:2 * side, :] = jnp.zeros((acc_ref.shape[0], 2 * side, side), f32)
        if with_diag:
            acc_ref[:, 2 * side:, :] = diag_ref[...]

    count = count_ref[0]

    @pl.when(step * per_block < count)
    def _():
        for k in range(per_block):
            slot = step * per_block + k
            ub = users_ref[slot]
            ib = items_ref[slot]
            user_rows = panel_ref[ub, 0:side, :]
            item_cols = panel_ref[ib, 3 * side:4 * side, :]
            predicted = jnp.dot(user_rows, item_cols, preferred_element_type=f32)
            residual_ref[k] = (weighted_ref[k].astype(f32) * (ratings_ref[k].astype(f32) - predicted)).astype(bf16)
        for k in range(per_block):
            slot = step * per_block + k
            ub = users_ref[slot]
            ib = items_ref[slot]
            residual = residual_ref[k]
            item_rows = panel_ref[ib, side:2 * side, :]
            user_cols = panel_ref[ub, 2 * side:3 * side, :]
            acc_ref[ub, 0:side, :] += jnp.dot(residual, item_rows, preferred_element_type=f32)
            acc_ref[ib, side:2 * side, :] += jnp.dot(user_cols, residual, preferred_element_type=f32)


def tile_terms(blocks, count, tile_users, tile_items, panel, ratings, weighted, diag=None):
    with_diag = diag is not None
    slots, side, _ = ratings.shape
    per_block = PER_BLOCK
    grid = slots // per_block
    acc_rows = 2 * side + (diag.shape[1] if with_diag else 0)

    def tile_map(step, count_ref, *_):
        last = jnp.maximum((count_ref[0] - 1) // per_block, 0)
        return (jnp.minimum(step, last), 0, 0)

    def whole(step, *_):
        return (0, 0, 0)

    in_specs = [
        pl.BlockSpec(panel.shape, whole),
        pl.BlockSpec((per_block, side, side), tile_map),
        pl.BlockSpec((per_block, side, side), tile_map),
    ]
    operands = [panel, ratings, weighted]
    if with_diag:
        in_specs.append(pl.BlockSpec(diag.shape, whole))
        operands.append(diag)
    flops = slots * (3 * 2 * side * side * side)
    bytes_accessed = 2 * ratings.size * 2 + panel.size * 2 + blocks * acc_rows * side * 4
    return pl.pallas_call(
        functools.partial(tile_kernel, with_diag, per_block),
        out_shape=jax.ShapeDtypeStruct((blocks, acc_rows, side), jnp.float32),
        grid_spec=pltpu.PrefetchScalarGridSpec(
            num_scalar_prefetch=3,
            grid=(grid,),
            in_specs=in_specs,
            out_specs=pl.BlockSpec((blocks, acc_rows, side), whole),
            scratch_shapes=[pltpu.VMEM((per_block, side, side), jnp.bfloat16)],
        ),
        compiler_params=pltpu.CompilerParams(dimension_semantics=("arbitrary",)),
        cost_estimate=pl.CostEstimate(flops=flops, bytes_accessed=bytes_accessed, transcendentals=0),
    )(count, tile_users, tile_items, *operands)


def prepare(weights, row_masks, tile_users, tile_items, tile_counts, blocks):
    f32 = jnp.float32
    slots, side, _ = weights.shape
    lanes = jnp.arange(side, dtype=jnp.int32)
    bits = jnp.bitwise_and(jnp.right_shift(row_masks[:, lanes // 32], lanes % 32), 1)
    live = (jnp.arange(slots, dtype=jnp.int32) < tile_counts[0]).astype(f32)
    keep = bits.astype(f32) * live[:, None]
    weighted = weights.astype(f32) * keep[:, :, None]
    row_sums = jnp.sum(weighted, axis=2)
    col_sums = jnp.sum(weighted, axis=1)
    ids = jnp.arange(blocks, dtype=jnp.int32)[:, None]
    user_hot = (tile_users[None, :] == ids).astype(f32)
    item_hot = (tile_items[None, :] == ids).astype(f32)
    user_diag = jnp.dot(user_hot, row_sums, precision=lax.Precision.HIGHEST)
    item_diag = jnp.dot(item_hot, col_sums, precision=lax.Precision.HIGHEST)
    diag = jnp.concatenate([user_diag[:, None], item_diag[:, None], jnp.zeros((blocks, 6, side), f32)], axis=1)
    return weighted.astype(jnp.bfloat16), diag


def gather_panel(users, items, blocks):
    own = jnp.concatenate([users.astype(jnp.bfloat16), items.astype(jnp.bfloat16)], axis=0)
    copies = jnp.broadcast_to(own[None], (blocks,) + own.shape)
    gathered = lax.all_to_all(copies, "item", 0, 0, tiled=False)
    return jnp.concatenate([gathered, jnp.swapaxes(gathered[:, :users.shape[0]], 1, 2),
                            jnp.swapaxes(gathered[:, users.shape[0]:], 1, 2)], axis=1)


def sum_over_user(part, groups):
    assert groups & (groups - 1) == 0
    distance = 1
    while distance < groups:
        pairs = [(j, j ^ distance) for j in range(groups)]
        part = part + lax.ppermute(part, "user", pairs)
        distance *= 2
    return part


def on_device(groups, blocks, ratings, weights, row_masks, tile_users, tile_items, tile_counts, users, items):
    side = ratings.shape[1]
    weighted, diag = prepare(weights, row_masks, tile_users, tile_items, tile_counts, blocks)
    user_weight = None
    item_weight = None
    for iteration in range(STEPS):
        with_diag = iteration == 0
        panel = gather_panel(users, items, blocks)
        acc = tile_terms(blocks, tile_counts, tile_users, tile_items, panel, ratings, weighted,
                         diag if with_diag else None)
        total = jnp.sum(lax.all_to_all(acc, "item", 0, 0, tiled=False), axis=0)
        item_total = sum_over_user(total[side:], groups)
        user_grad = total[0:side]
        item_grad = item_total[0:side].T
        if with_diag:
            user_weight = 2.0 * side + total[2 * side]
            item_weight = 2.0 * side + item_total[side + 1]
        users = users + STEP_SCALE * (user_grad / user_weight[:, None] - DECAY_RATE * users)
        items = items + STEP_SCALE * (item_grad / item_weight[:, None] - DECAY_RATE * items)
    return (users, items)


def solution(mesh):
    groups = mesh.shape["user"]
    blocks = mesh.shape["item"]
    return jax.shard_map(
        functools.partial(on_device, groups, blocks),
        mesh=mesh,
        in_specs=(
            P(("user", "item"), None, None),
            P(("user", "item"), None, None),
            P(("user", "item"), None),
            P(("user", "item")),
            P(("user", "item")),
            P(("user", "item")),
            P(("user", "item"), None),
            P("item", None),
        ),
        out_specs=(P(("user", "item"), None), P("item", None)),
        check_vma=False,
    )
```

```python
import functools

import jax
import jax.numpy as jnp
from jax import lax
from jax.experimental import pallas as pl
from jax.experimental.pallas import tpu as pltpu
from jax.sharding import PartitionSpec as P

STEPS = 2


STEP_SCALE = 4.0
DECAY_RATE = 0.02

PER_BLOCK = 40


def tile_kernel(with_diag, per_block, count_ref, users_ref, items_ref, *refs):
    if with_diag:
        panel_ref, ratings_ref, weighted_ref, diag_ref, acc_ref, residual_ref = refs
    else:
        panel_ref, ratings_ref, weighted_ref, acc_ref, residual_ref = refs
    step = pl.program_id(0)
    side = ratings_ref.shape[1]
    f32, bf16 = jnp.float32, jnp.bfloat16

    @pl.when(step == 0)
    def _():
        acc_ref[:, 0:2 * side, :] = jnp.zeros((acc_ref.shape[0], 2 * side, side), f32)
        if with_diag:
            acc_ref[:, 2 * side:, :] = diag_ref[...]

    count = count_ref[0]

    @pl.when(step * per_block < count)
    def _():
        for k in range(per_block):
            slot = step * per_block + k
            ub = users_ref[slot]
            ib = items_ref[slot]
            user_rows = panel_ref[ub, 0:side, :]
            item_cols = panel_ref[ib, 3 * side:4 * side, :]
            predicted = jnp.dot(user_rows, item_cols, preferred_element_type=f32)
            residual_ref[k] = (weighted_ref[k].astype(f32) * (ratings_ref[k].astype(f32) - predicted)).astype(bf16)
        for k in range(per_block):
            slot = step * per_block + k
            ub = users_ref[slot]
            ib = items_ref[slot]
            residual = residual_ref[k]
            item_rows = panel_ref[ib, side:2 * side, :]
            user_cols = panel_ref[ub, 2 * side:3 * side, :]
            acc_ref[ub, 0:side, :] += jnp.dot(residual, item_rows, preferred_element_type=f32)
            acc_ref[ib, side:2 * side, :] += jnp.dot(user_cols, residual, preferred_element_type=f32)


def tile_terms(blocks, count, tile_users, tile_items, panel, ratings, weighted, diag=None):
    with_diag = diag is not None
    slots, side, _ = ratings.shape
    per_block = PER_BLOCK
    grid = slots // per_block
    acc_rows = 2 * side + (diag.shape[1] if with_diag else 0)

    def tile_map(step, count_ref, *_):
        last = jnp.maximum((count_ref[0] - 1) // per_block, 0)
        return (jnp.minimum(step, last), 0, 0)

    def whole(step, *_):
        return (0, 0, 0)

    in_specs = [
        pl.BlockSpec(panel.shape, whole),
        pl.BlockSpec((per_block, side, side), tile_map),
        pl.BlockSpec((per_block, side, side), tile_map),
    ]
    operands = [panel, ratings, weighted]
    if with_diag:
        in_specs.append(pl.BlockSpec(diag.shape, whole))
        operands.append(diag)
    flops = slots * (3 * 2 * side * side * side)
    bytes_accessed = 2 * ratings.size * 2 + panel.size * 2 + blocks * acc_rows * side * 4
    return pl.pallas_call(
        functools.partial(tile_kernel, with_diag, per_block),
        out_shape=jax.ShapeDtypeStruct((blocks, acc_rows, side), jnp.float32),
        grid_spec=pltpu.PrefetchScalarGridSpec(
            num_scalar_prefetch=3,
            grid=(grid,),
            in_specs=in_specs,
            out_specs=pl.BlockSpec((blocks, acc_rows, side), whole),
            scratch_shapes=[pltpu.VMEM((per_block, side, side), jnp.bfloat16)],
        ),
        compiler_params=pltpu.CompilerParams(dimension_semantics=("arbitrary",)),
        cost_estimate=pl.CostEstimate(flops=flops, bytes_accessed=bytes_accessed, transcendentals=0),
    )(count, tile_users, tile_items, *operands)


def prepare(weights, row_masks, tile_users, tile_items, tile_counts, blocks):
    f32 = jnp.float32
    slots, side, _ = weights.shape
    lanes = jnp.arange(side, dtype=jnp.int32)
    bits = jnp.bitwise_and(jnp.right_shift(row_masks[:, lanes // 32], lanes % 32), 1)
    live = (jnp.arange(slots, dtype=jnp.int32) < tile_counts[0]).astype(f32)
    keep = bits.astype(f32) * live[:, None]
    weighted = weights.astype(f32) * keep[:, :, None]
    row_sums = jnp.sum(weighted, axis=2)
    col_sums = jnp.sum(weighted, axis=1)
    ids = jnp.arange(blocks, dtype=jnp.int32)[:, None]
    user_hot = (tile_users[None, :] == ids).astype(f32)
    item_hot = (tile_items[None, :] == ids).astype(f32)
    user_diag = jnp.dot(user_hot, row_sums, precision=lax.Precision.HIGHEST)
    item_diag = jnp.dot(item_hot, col_sums, precision=lax.Precision.HIGHEST)
    diag = jnp.concatenate([user_diag[:, None], item_diag[:, None], jnp.zeros((blocks, 6, side), f32)], axis=1)
    return weighted.astype(jnp.bfloat16), diag


def gather_panel(users, items, blocks):
    own = jnp.concatenate([users.astype(jnp.bfloat16), items.astype(jnp.bfloat16)], axis=0)
    copies = jnp.broadcast_to(own[None], (blocks,) + own.shape)
    gathered = lax.all_to_all(copies, "item", 0, 0, tiled=False)
    return jnp.concatenate([gathered, jnp.swapaxes(gathered[:, :users.shape[0]], 1, 2),
                            jnp.swapaxes(gathered[:, users.shape[0]:], 1, 2)], axis=1)


def user_rounds(groups):
    rounds = []
    distance = 1
    while distance < groups:
        rounds.append([j ^ distance for j in range(groups)])
        distance *= 2
    if groups != 16:
        return rounds

    def across(j):
        z = j // 2
        far = (6 - z) % 8 if z % 2 == 0 else (8 - z) % 8
        return far * 2 + j % 2

    return [rounds[0], rounds[2], [across(j) for j in range(groups)], rounds[1]]


def sum_over_user(part, groups):
    assert groups & (groups - 1) == 0
    for partner in user_rounds(groups):
        pairs = [(j, partner[j]) for j in range(groups)]
        part = part + lax.ppermute(part, "user", pairs)
    return part


def on_device(groups, blocks, ratings, weights, row_masks, tile_users, tile_items, tile_counts, users, items):
    side = ratings.shape[1]
    weighted, diag = prepare(weights, row_masks, tile_users, tile_items, tile_counts, blocks)
    user_weight = None
    item_weight = None
    for iteration in range(STEPS):
        with_diag = iteration == 0
        panel = gather_panel(users, items, blocks)
        acc = tile_terms(blocks, tile_counts, tile_users, tile_items, panel, ratings, weighted,
                         diag if with_diag else None)
        total = jnp.sum(lax.all_to_all(acc, "item", 0, 0, tiled=False), axis=0)
        item_total = sum_over_user(total[side:], groups)
        user_grad = total[0:side]
        item_grad = item_total[0:side].T
        if with_diag:
            user_weight = 2.0 * side + total[2 * side]
            item_weight = 2.0 * side + item_total[side + 1]
        users = users + STEP_SCALE * (user_grad / user_weight[:, None] - DECAY_RATE * users)
        items = items + STEP_SCALE * (item_grad / item_weight[:, None] - DECAY_RATE * items)
    return (users, items)


def solution(mesh):
    groups = mesh.shape["user"]
    blocks = mesh.shape["item"]
    return jax.shard_map(
        functools.partial(on_device, groups, blocks),
        mesh=mesh,
        in_specs=(
            P(("user", "item"), None, None),
            P(("user", "item"), None, None),
            P(("user", "item"), None),
            P(("user", "item")),
            P(("user", "item")),
            P(("user", "item")),
            P(("user", "item"), None),
            P("item", None),
        ),
        out_specs=(P(("user", "item"), None), P("item", None)),
        check_vma=False,
    )
```

```python
import functools

import jax
import jax.numpy as jnp
from jax import lax
from jax.experimental import pallas as pl
from jax.experimental.pallas import tpu as pltpu
from jax.sharding import PartitionSpec as P

STEPS = 2


STEP_SCALE = 4.0
DECAY_RATE = 0.02

PER_BLOCK = 40


def tile_kernel(with_diag, per_block, count_ref, users_ref, items_ref, *refs):
    if with_diag:
        panel_ref, flip_ref, ratings_ref, weighted_ref, diag_ref, acc_ref, residual_ref = refs
    else:
        panel_ref, flip_ref, ratings_ref, weighted_ref, acc_ref, residual_ref = refs
    step = pl.program_id(0)
    side = ratings_ref.shape[1]
    f32, bf16 = jnp.float32, jnp.bfloat16

    @pl.when(step == 0)
    def _():
        acc_ref[:, 0:2 * side, :] = jnp.zeros((acc_ref.shape[0], 2 * side, side), f32)
        if with_diag:
            acc_ref[:, 2 * side:, :] = diag_ref[...]

    count = count_ref[0]

    @pl.when(step * per_block < count)
    def _():
        for k in range(per_block):
            slot = step * per_block + k
            ub = users_ref[slot]
            ib = items_ref[slot]
            user_rows = panel_ref[ub, 0:side, :]
            item_cols = flip_ref[ib, :, side:2 * side]
            predicted = jnp.dot(user_rows, item_cols, preferred_element_type=f32)
            residual_ref[k] = (weighted_ref[k].astype(f32) * (ratings_ref[k].astype(f32) - predicted)).astype(bf16)
        for k in range(per_block):
            slot = step * per_block + k
            ub = users_ref[slot]
            ib = items_ref[slot]
            residual = residual_ref[k]
            item_rows = panel_ref[ib, side:2 * side, :]
            user_cols = flip_ref[ub, :, 0:side]
            acc_ref[ub, 0:side, :] += jnp.dot(residual, item_rows, preferred_element_type=f32)
            acc_ref[ib, side:2 * side, :] += jnp.dot(user_cols, residual, preferred_element_type=f32)


def tile_terms(blocks, count, tile_users, tile_items, panel, flip, ratings, weighted, diag=None):
    with_diag = diag is not None
    slots, side, _ = ratings.shape
    per_block = PER_BLOCK
    grid = slots // per_block
    acc_rows = 2 * side + (diag.shape[1] if with_diag else 0)

    def tile_map(step, count_ref, *_):
        last = jnp.maximum((count_ref[0] - 1) // per_block, 0)
        return (jnp.minimum(step, last), 0, 0)

    def whole(step, *_):
        return (0, 0, 0)

    in_specs = [
        pl.BlockSpec(panel.shape, whole),
        pl.BlockSpec(flip.shape, whole),
        pl.BlockSpec((per_block, side, side), tile_map),
        pl.BlockSpec((per_block, side, side), tile_map),
    ]
    operands = [panel, flip, ratings, weighted]
    if with_diag:
        in_specs.append(pl.BlockSpec(diag.shape, whole))
        operands.append(diag)
    flops = slots * (3 * 2 * side * side * side)
    bytes_accessed = 2 * ratings.size * 2 + 2 * panel.size * 2 + blocks * acc_rows * side * 4
    return pl.pallas_call(
        functools.partial(tile_kernel, with_diag, per_block),
        out_shape=jax.ShapeDtypeStruct((blocks, acc_rows, side), jnp.float32),
        grid_spec=pltpu.PrefetchScalarGridSpec(
            num_scalar_prefetch=3,
            grid=(grid,),
            in_specs=in_specs,
            out_specs=pl.BlockSpec((blocks, acc_rows, side), whole),
            scratch_shapes=[pltpu.VMEM((per_block, side, side), jnp.bfloat16)],
        ),
        compiler_params=pltpu.CompilerParams(dimension_semantics=("arbitrary",)),
        cost_estimate=pl.CostEstimate(flops=flops, bytes_accessed=bytes_accessed, transcendentals=0),
    )(count, tile_users, tile_items, *operands)


def prepare(weights, row_masks, tile_users, tile_items, tile_counts, blocks):
    f32 = jnp.float32
    slots, side, _ = weights.shape
    lanes = jnp.arange(side, dtype=jnp.int32)
    bits = jnp.bitwise_and(jnp.right_shift(row_masks[:, lanes // 32], lanes % 32), 1)
    live = (jnp.arange(slots, dtype=jnp.int32) < tile_counts[0]).astype(f32)
    keep = bits.astype(f32) * live[:, None]
    weighted = weights.astype(f32) * keep[:, :, None]
    row_sums = jnp.sum(weighted, axis=2)
    col_sums = jnp.sum(weighted, axis=1)
    ids = jnp.arange(blocks, dtype=jnp.int32)[:, None]
    user_hot = (tile_users[None, :] == ids).astype(f32)
    item_hot = (tile_items[None, :] == ids).astype(f32)
    user_diag = jnp.dot(user_hot, row_sums, precision=lax.Precision.HIGHEST)
    item_diag = jnp.dot(item_hot, col_sums, precision=lax.Precision.HIGHEST)
    diag = jnp.concatenate([user_diag[:, None], item_diag[:, None], jnp.zeros((blocks, 6, side), f32)], axis=1)
    return weighted.astype(jnp.bfloat16), diag


def gather_panel(users, items, blocks):
    own = jnp.concatenate([users.astype(jnp.bfloat16), items.astype(jnp.bfloat16)], axis=0)
    copies = jnp.broadcast_to(own[None], (blocks,) + own.shape)
    gathered = lax.all_to_all(copies, "item", 0, 0, tiled=False)
    return gathered, jnp.swapaxes(gathered, 1, 2)


def user_rounds(groups):
    rounds = []
    distance = 1
    while distance < groups:
        rounds.append([j ^ distance for j in range(groups)])
        distance *= 2
    if groups != 16:
        return rounds

    def across(j):
        z = j // 2
        far = (6 - z) % 8 if z % 2 == 0 else (8 - z) % 8
        return far * 2 + j % 2

    return [rounds[0], rounds[2], [across(j) for j in range(groups)], rounds[1]]


def sum_over_user(part, groups):
    assert groups & (groups - 1) == 0
    for partner in user_rounds(groups):
        pairs = [(j, partner[j]) for j in range(groups)]
        part = part + lax.ppermute(part, "user", pairs)
    return part


def on_device(groups, blocks, ratings, weights, row_masks, tile_users, tile_items, tile_counts, users, items):
    side = ratings.shape[1]
    weighted, diag = prepare(weights, row_masks, tile_users, tile_items, tile_counts, blocks)
    user_weight = None
    item_weight = None
    for iteration in range(STEPS):
        with_diag = iteration == 0
        panel, flip = gather_panel(users, items, blocks)
        acc = tile_terms(blocks, tile_counts, tile_users, tile_items, panel, flip, ratings, weighted,
                         diag if with_diag else None)
        total = jnp.sum(lax.all_to_all(acc, "item", 0, 0, tiled=False), axis=0)
        item_total = sum_over_user(total[side:], groups)
        user_grad = total[0:side]
        item_grad = item_total[0:side].T
        if with_diag:
            user_weight = 2.0 * side + total[2 * side]
            item_weight = 2.0 * side + item_total[side + 1]
        users = users + STEP_SCALE * (user_grad / user_weight[:, None] - DECAY_RATE * users)
        items = items + STEP_SCALE * (item_grad / item_weight[:, None] - DECAY_RATE * items)
    return (users, items)


def solution(mesh):
    groups = mesh.shape["user"]
    blocks = mesh.shape["item"]
    return jax.shard_map(
        functools.partial(on_device, groups, blocks),
        mesh=mesh,
        in_specs=(
            P(("user", "item"), None, None),
            P(("user", "item"), None, None),
            P(("user", "item"), None),
            P(("user", "item")),
            P(("user", "item")),
            P(("user", "item")),
            P(("user", "item"), None),
            P("item", None),
        ),
        out_specs=(P(("user", "item"), None), P("item", None)),
        check_vma=False,
    )
```

```python
import functools

import jax
import jax.numpy as jnp
from jax import lax
from jax.experimental import pallas as pl
from jax.experimental.pallas import tpu as pltpu
from jax.sharding import PartitionSpec as P

STEPS = 2


STEP_SCALE = 4.0
DECAY_RATE = 0.02

PER_BLOCK = 60


def tile_kernel(with_diag, per_block, count_ref, users_ref, items_ref, *refs):
    if with_diag:
        panel_ref, flip_ref, ratings_ref, weighted_ref, diag_ref, acc_ref, residual_ref = refs
    else:
        panel_ref, flip_ref, ratings_ref, weighted_ref, acc_ref, residual_ref = refs
    step = pl.program_id(0)
    side = ratings_ref.shape[1]
    f32, bf16 = jnp.float32, jnp.bfloat16

    @pl.when(step == 0)
    def _():
        acc_ref[:, 0:2 * side, :] = jnp.zeros((acc_ref.shape[0], 2 * side, side), f32)
        if with_diag:
            acc_ref[:, 2 * side:, :] = diag_ref[...]

    count = count_ref[0]

    @pl.when(step * per_block < count)
    def _():
        for k in range(per_block):
            slot = step * per_block + k
            ub = users_ref[slot]
            ib = items_ref[slot]
            user_rows = panel_ref[ub, 0:side, :]
            item_cols = flip_ref[ib, :, side:2 * side]
            predicted = jnp.dot(user_rows, item_cols, preferred_element_type=f32)
            residual_ref[k] = (weighted_ref[k].astype(f32) * (ratings_ref[k].astype(f32) - predicted)).astype(bf16)
        for k in range(per_block):
            slot = step * per_block + k
            ub = users_ref[slot]
            ib = items_ref[slot]
            residual = residual_ref[k]
            item_rows = panel_ref[ib, side:2 * side, :]
            user_cols = flip_ref[ub, :, 0:side]
            acc_ref[ub, 0:side, :] += jnp.dot(residual, item_rows, preferred_element_type=f32)
            acc_ref[ib, side:2 * side, :] += jnp.dot(user_cols, residual, preferred_element_type=f32)


def tile_terms(blocks, count, tile_users, tile_items, panel, flip, ratings, weighted, diag=None):
    with_diag = diag is not None
    slots, side, _ = ratings.shape
    per_block = PER_BLOCK
    grid = slots // per_block
    acc_rows = 2 * side + (diag.shape[1] if with_diag else 0)

    def tile_map(step, count_ref, *_):
        last = jnp.maximum((count_ref[0] - 1) // per_block, 0)
        return (jnp.minimum(step, last), 0, 0)

    def whole(step, *_):
        return (0, 0, 0)

    in_specs = [
        pl.BlockSpec(panel.shape, whole),
        pl.BlockSpec(flip.shape, whole),
        pl.BlockSpec((per_block, side, side), tile_map),
        pl.BlockSpec((per_block, side, side), tile_map),
    ]
    operands = [panel, flip, ratings, weighted]
    if with_diag:
        in_specs.append(pl.BlockSpec(diag.shape, whole))
        operands.append(diag)
    flops = slots * (3 * 2 * side * side * side)
    bytes_accessed = 2 * ratings.size * 2 + 2 * panel.size * 2 + blocks * acc_rows * side * 4
    return pl.pallas_call(
        functools.partial(tile_kernel, with_diag, per_block),
        out_shape=jax.ShapeDtypeStruct((blocks, acc_rows, side), jnp.float32),
        grid_spec=pltpu.PrefetchScalarGridSpec(
            num_scalar_prefetch=3,
            grid=(grid,),
            in_specs=in_specs,
            out_specs=pl.BlockSpec((blocks, acc_rows, side), whole),
            scratch_shapes=[pltpu.VMEM((per_block, side, side), jnp.bfloat16)],
        ),
        compiler_params=pltpu.CompilerParams(dimension_semantics=("arbitrary",)),
        cost_estimate=pl.CostEstimate(flops=flops, bytes_accessed=bytes_accessed, transcendentals=0),
    )(count, tile_users, tile_items, *operands)


def prepare(weights, row_masks, tile_users, tile_items, tile_counts, blocks):
    f32 = jnp.float32
    slots, side, _ = weights.shape
    lanes = jnp.arange(side, dtype=jnp.int32)
    bits = jnp.bitwise_and(jnp.right_shift(row_masks[:, lanes // 32], lanes % 32), 1)
    live = (jnp.arange(slots, dtype=jnp.int32) < tile_counts[0]).astype(f32)
    keep = bits.astype(f32) * live[:, None]
    weighted = weights.astype(f32) * keep[:, :, None]
    row_sums = jnp.sum(weighted, axis=2)
    col_sums = jnp.sum(weighted, axis=1)
    ids = jnp.arange(blocks, dtype=jnp.int32)[:, None]
    user_hot = (tile_users[None, :] == ids).astype(f32)
    item_hot = (tile_items[None, :] == ids).astype(f32)
    user_diag = jnp.dot(user_hot, row_sums, precision=lax.Precision.HIGHEST)
    item_diag = jnp.dot(item_hot, col_sums, precision=lax.Precision.HIGHEST)
    diag = jnp.concatenate([user_diag[:, None], item_diag[:, None], jnp.zeros((blocks, 6, side), f32)], axis=1)
    return weighted.astype(jnp.bfloat16), diag


def gather_panel(users, items, blocks):
    own = jnp.concatenate([users.astype(jnp.bfloat16), items.astype(jnp.bfloat16)], axis=0)
    copies = jnp.broadcast_to(own[None], (blocks,) + own.shape)
    gathered = lax.all_to_all(copies, "item", 0, 0, tiled=False)
    return gathered, jnp.swapaxes(gathered, 1, 2)


def user_rounds(groups):
    rounds = []
    distance = 1
    while distance < groups:
        rounds.append([j ^ distance for j in range(groups)])
        distance *= 2
    if groups != 16:
        return rounds

    def across(j):
        z = j // 2
        far = (6 - z) % 8 if z % 2 == 0 else (8 - z) % 8
        return far * 2 + j % 2

    return [rounds[0], rounds[2], [across(j) for j in range(groups)], rounds[1]]


def sum_over_user(part, groups):
    assert groups & (groups - 1) == 0
    for partner in user_rounds(groups):
        pairs = [(j, partner[j]) for j in range(groups)]
        part = part + lax.ppermute(part, "user", pairs)
    return part


def on_device(groups, blocks, ratings, weights, row_masks, tile_users, tile_items, tile_counts, users, items):
    side = ratings.shape[1]
    weighted, diag = prepare(weights, row_masks, tile_users, tile_items, tile_counts, blocks)
    user_weight = None
    item_weight = None
    for iteration in range(STEPS):
        with_diag = iteration == 0
        panel, flip = gather_panel(users, items, blocks)
        acc = tile_terms(blocks, tile_counts, tile_users, tile_items, panel, flip, ratings, weighted,
                         diag if with_diag else None)
        total = jnp.sum(lax.all_to_all(acc, "item", 0, 0, tiled=False), axis=0)
        item_total = sum_over_user(total[side:], groups)
        user_grad = total[0:side]
        item_grad = item_total[0:side].T
        if with_diag:
            user_weight = 2.0 * side + total[2 * side]
            item_weight = 2.0 * side + item_total[side + 1]
        users = users + STEP_SCALE * (user_grad / user_weight[:, None] - DECAY_RATE * users)
        items = items + STEP_SCALE * (item_grad / item_weight[:, None] - DECAY_RATE * items)
    return (users, items)


def solution(mesh):
    groups = mesh.shape["user"]
    blocks = mesh.shape["item"]
    return jax.shard_map(
        functools.partial(on_device, groups, blocks),
        mesh=mesh,
        in_specs=(
            P(("user", "item"), None, None),
            P(("user", "item"), None, None),
            P(("user", "item"), None),
            P(("user", "item")),
            P(("user", "item")),
            P(("user", "item")),
            P(("user", "item"), None),
            P("item", None),
        ),
        out_specs=(P(("user", "item"), None), P("item", None)),
        check_vma=False,
    )
```
